256 devices in a mesh: row: 32 (over y_hi, z, core), col: 8 (over x, y_lo).
Axes of the slice: x: 4, y: 4 (y_hi: 2, y_lo: 2; y = y_hi * 2 + y_lo), z: 8, core: 2. Of those that a mesh axis runs over, the one named last changes fastest.
Arguments:
- weight: bfloat16 [16384, 16384], P('row', 'col'), may hold values from -20 to 20, as said below
- panel_index: int32 [1], replicated, may hold values from 0 to 15
Outputs:
- updated_panel: bfloat16 [16384, 1024], P('row', 'col')
- gram_rows: float32 [1024, 16384], P('row', 'col')
The draws below stay inside these ranges and needn't reach their ends.
Inputs may be any that keep to these rules, and one draw needn't show every extreme that they name: `weight`: entries are real-valued and independent, with column and row scales that differ from column to column and row to row.
All inputs are finite; a program needn't handle non-finite values.
Results may differ from the reference program's by a relative error of at most 0.0055.
Values may be sent and summed in bfloat16 or wider, within the bound.
No kernel may reach another device: no remote copies, remote signals or barrier semaphores. Data moves between devices by JAX's collectives and lax.ppermute only.
A program may use at most 64 MiB of HBM per device.

```python
import math
import jax
import jax.numpy as jnp
from jax import lax

M = 16384
N = 16384
PANEL = 1024


def draw_weight(key, part):
    key_base, key_col, key_row = jax.random.split(key, 3)
    col_scales = jnp.exp(jax.random.uniform(key_col, (1, N), jnp.float32, math.log(0.6), math.log(1.8)))
    row_scales = jnp.exp(jax.random.uniform(key_row, (M, 1), jnp.float32, math.log(0.7), math.log(1.4)))
    base = jnp.clip(jax.random.normal(key_base, (M, N), jnp.float32), -6.0, 6.0)
    return (base * row_scales * col_scales).astype(jnp.bfloat16)


def setup_inputs(seed: int = 0) -> dict:
    key_of = jax.random.split(jax.random.key(seed), 3)
    weight = draw_weight(jax.random.fold_in(key_of[2], 71), 0)
    panel_index = jax.random.randint(key_of[1], (1,), 0, N // PANEL).astype(jnp.int32)
    return {"weight": weight, "panel_index": panel_index}


def reference(weight, panel_index):
    begin_col = (panel_index[0] * PANEL).astype(jnp.int32)
    panel_cols = lax.dynamic_slice_in_dim(weight, begin_col, PANEL, 1)
    gram_rows = lax.dot_general(panel_cols, weight, (((0,), (0,)), ((), ())), preferred_element_type=jnp.float32) * (1.0 / M)
    gram_half = gram_rows.astype(jnp.bfloat16)
    product = lax.dot_general(weight, gram_half, (((1,), (1,)), ((), ())), preferred_element_type=jnp.float32)
    updated_panel = (1.5 * panel_cols.astype(jnp.float32) - 0.5 * product).astype(jnp.bfloat16)
    return updated_panel, gram_rows
```

```python
import jax
import jax.numpy as jnp
from jax import lax
from jax.sharding import PartitionSpec as P, Mesh

M = 16384
PANEL = 1024
CFG = {"order": ("c","z","yh"), "mode": {"c":"pp","z":"pp","yh":"pp"}}

ROW = ("yh", "z", "c")
COL = ("x", "yl")


def pair_rs(x, axis):
    k = lax.axis_index(axis)
    h = x.shape[0] // 2
    keep = lax.dynamic_slice_in_dim(x, k * h, h, 0)
    send = lax.dynamic_slice_in_dim(x, (1 - k) * h, h, 0)
    return keep + lax.ppermute(send, axis, [(0, 1), (1, 0)])


def pair_ag(x, axis):
    k = lax.axis_index(axis)
    got = lax.ppermute(x, axis, [(0, 1), (1, 0)])
    return jnp.where(k == 0, jnp.concatenate([x, got], 0), jnp.concatenate([got, x], 0))


def ring_rs(x, axis):
    n = lax.axis_size(axis)
    d = lax.axis_index(axis)
    h = x.shape[0] // n
    piece = lambda k: lax.dynamic_slice_in_dim(x, (k % n) * h, h, 0)
    fw = [(i, (i + 1) % n) for i in range(n)]
    bw = [(i, (i - 1) % n) for i in range(n)]
    ncw = n // 2
    nccw = n - 1 - ncw
    acc_cw = piece(d + ncw)
    acc_ccw = piece(d - nccw)
    for s in range(ncw):
        acc_cw = lax.ppermute(acc_cw, axis, fw)
        if s < nccw:
            acc_ccw = lax.ppermute(acc_ccw, axis, bw)
        if s < ncw - 1:
            acc_cw = acc_cw + piece(d + ncw - s - 1)
        if s < nccw - 1:
            acc_ccw = acc_ccw + piece(d - nccw + s + 1)
    return acc_cw + acc_ccw + piece(d)


def ring_ag(x, axis):
    n = lax.axis_size(axis)
    d = lax.axis_index(axis)
    h = x.shape[0]
    fw = [(i, (i + 1) % n) for i in range(n)]
    bw = [(i, (i - 1) % n) for i in range(n)]
    out = jnp.zeros((n * h,) + x.shape[1:], x.dtype)
    out = lax.dynamic_update_slice_in_dim(out, x, d * h, 0)
    ncw = n // 2
    nccw = n - 1 - ncw
    a = x
    b = x
    for s in range(ncw):
        a = lax.ppermute(a, axis, fw)
        out = lax.dynamic_update_slice_in_dim(out, a, ((d - s - 1) % n) * h, 0)
        if s < nccw:
            b = lax.ppermute(b, axis, bw)
            out = lax.dynamic_update_slice_in_dim(out, b, ((d + s + 1) % n) * h, 0)
    return out


def rs(x, axis, mode):
    if mode == "sc":
        return lax.psum_scatter(x, axis, scatter_dimension=0, tiled=True)
    if lax.axis_size(axis) == 2:
        return pair_rs(x, axis)
    return ring_rs(x, axis)


def ag(x, axis, mode):
    if mode == "sc":
        return lax.all_gather(x, axis, axis=0, tiled=True)
    if lax.axis_size(axis) == 2:
        return pair_ag(x, axis)
    return ring_ag(x, axis)


def broadcast(shard, root):
    mine = lax.axis_index(COL) == root
    t = jnp.where(mine, shard, jnp.zeros_like(shard)).T
    t = rs(t, "x", "pp")
    t = rs(t, "yl", "pp")
    t = ag(t, "yl", "pp")
    t = ag(t, "x", "pp")
    return t.T


def on_device(weight, panel_index):
    local_cols = weight.shape[1]
    begin_col = panel_index[0] * PANEL
    owner_col = begin_col // local_cols
    offset_col = begin_col % local_cols
    own_block = lax.dynamic_slice_in_dim(weight, offset_col, PANEL, 1)
    panel_cols = broadcast(own_block, owner_col)
    order = CFG["order"]
    sizes = {a: lax.axis_size(a) for a in ROW}
    shape = [sizes[a] for a in ROW] + [PANEL // lax.axis_size(ROW)]
    perm = [ROW.index(a) for a in order] + [3]
    p5 = panel_cols.reshape((panel_cols.shape[0],) + tuple(shape))
    p_perm = jnp.transpose(p5, [0] + [q + 1 for q in perm]).reshape(panel_cols.shape)
    part = lax.dot_general(p_perm, weight, (((0,), (0,)), ((), ())), preferred_element_type=jnp.float32) * (1.0 / M)
    x = part
    for a in order:
        x = rs(x, a, CFG["mode"][a])
    gram_rows = x
    g = gram_rows.astype(jnp.bfloat16)
    for a in reversed(order):
        g = ag(g, a, CFG["mode"][a])
    inv = [perm.index(q) for q in range(4)]
    g5 = g.reshape(tuple(shape[q] for q in perm) + (g.shape[1],))
    gram_half = jnp.transpose(g5, inv + [4]).reshape(g.shape)
    partial_t = lax.dot_general(gram_half, weight, (((1,), (1,)), ((), ())), preferred_element_type=jnp.float32)
    summed = rs(rs(partial_t, "x", "pp"), "yl", "pp").T
    col_width = PANEL // lax.axis_size(COL)
    own_cols = lax.dynamic_slice_in_dim(panel_cols, lax.axis_index(COL) * col_width, col_width, 1)
    updated_panel = (1.5 * own_cols.astype(jnp.float32) - 0.5 * summed).astype(jnp.bfloat16)
    return (updated_panel, gram_rows)


def solution(mesh):
    m5 = Mesh(mesh.devices.reshape(2, 8, 2, 4, 2), ROW + COL)
    return jax.shard_map(on_device, mesh=m5, in_specs=(P(ROW, COL), P()),
                         out_specs=(P(ROW, COL), P(ROW, COL)), check_vma=False)
```

```python
import jax
import jax.numpy as jnp
from jax import lax
from jax.sharding import PartitionSpec as P, Mesh

M = 16384
PANEL = 1024
CFG = {'chunks': 2, "order": ("c","z","yh"), "mode": {"c":"pp","z":"pp","yh":"pp"}}

ROW = ("yh", "z", "c")
COL = ("x", "yl")


def pair_rs(x, axis):
    k = lax.axis_index(axis)
    h = x.shape[0] // 2
    keep = lax.dynamic_slice_in_dim(x, k * h, h, 0)
    send = lax.dynamic_slice_in_dim(x, (1 - k) * h, h, 0)
    return keep + lax.ppermute(send, axis, [(0, 1), (1, 0)])


def pair_ag(x, axis):
    k = lax.axis_index(axis)
    got = lax.ppermute(x, axis, [(0, 1), (1, 0)])
    return jnp.where(k == 0, jnp.concatenate([x, got], 0), jnp.concatenate([got, x], 0))


def ring_rs(x, axis):
    n = lax.axis_size(axis)
    d = lax.axis_index(axis)
    h = x.shape[0] // n
    piece = lambda k: lax.dynamic_slice_in_dim(x, (k % n) * h, h, 0)
    fw = [(i, (i + 1) % n) for i in range(n)]
    bw = [(i, (i - 1) % n) for i in range(n)]
    ncw = n // 2
    nccw = n - 1 - ncw
    acc_cw = piece(d + ncw)
    acc_ccw = piece(d - nccw)
    for s in range(ncw):
        acc_cw = lax.ppermute(acc_cw, axis, fw)
        if s < nccw:
            acc_ccw = lax.ppermute(acc_ccw, axis, bw)
        if s < ncw - 1:
            acc_cw = acc_cw + piece(d + ncw - s - 1)
        if s < nccw - 1:
            acc_ccw = acc_ccw + piece(d - nccw + s + 1)
    return acc_cw + acc_ccw + piece(d)


def ring_ag(x, axis):
    n = lax.axis_size(axis)
    d = lax.axis_index(axis)
    h = x.shape[0]
    fw = [(i, (i + 1) % n) for i in range(n)]
    bw = [(i, (i - 1) % n) for i in range(n)]
    out = jnp.zeros((n * h,) + x.shape[1:], x.dtype)
    out = lax.dynamic_update_slice_in_dim(out, x, d * h, 0)
    ncw = n // 2
    nccw = n - 1 - ncw
    a = x
    b = x
    for s in range(ncw):
        a = lax.ppermute(a, axis, fw)
        out = lax.dynamic_update_slice_in_dim(out, a, ((d - s - 1) % n) * h, 0)
        if s < nccw:
            b = lax.ppermute(b, axis, bw)
            out = lax.dynamic_update_slice_in_dim(out, b, ((d + s + 1) % n) * h, 0)
    return out


def rs(x, axis, mode):
    if mode == "sc":
        return lax.psum_scatter(x, axis, scatter_dimension=0, tiled=True)
    if lax.axis_size(axis) == 2:
        return pair_rs(x, axis)
    return ring_rs(x, axis)


def ag(x, axis, mode):
    if mode == "sc":
        return lax.all_gather(x, axis, axis=0, tiled=True)
    if lax.axis_size(axis) == 2:
        return pair_ag(x, axis)
    return ring_ag(x, axis)


def broadcast_t(t, root):
    mine = lax.axis_index(COL) == root
    t = jnp.where(mine, t, jnp.zeros_like(t))
    t = rs(t, "x", "pp")
    t = rs(t, "yl", "pp")
    t = ag(t, "yl", "pp")
    return ag(t, "x", "pp")


def on_device(weight, panel_index):
    local_cols = weight.shape[1]
    begin_col = panel_index[0] * PANEL
    owner_col = begin_col // local_cols
    offset_col = begin_col % local_cols
    own_block = lax.dynamic_slice_in_dim(weight, offset_col, PANEL, 1)
    n_row = lax.axis_size(ROW)
    n_col = lax.axis_size(COL)
    rows_per = PANEL // n_row
    chunks = CFG["chunks"]
    jw = rows_per // chunks
    order = CFG["order"]
    sizes = {a: lax.axis_size(a) for a in ROW}
    perm = [ROW.index(a) for a in order]
    inv = [perm.index(q) for q in range(3)]
    rshape = [sizes[a] for a in ROW]
    blk = own_block.T.reshape(n_row, rows_per, own_block.shape[0])
    grams = []
    upds = []
    for k in range(chunks):
        pk = blk[:, k * jw:(k + 1) * jw, :].reshape(n_row * jw, own_block.shape[0])
        pk = broadcast_t(pk, owner_col)
        p5 = pk.reshape(rshape + [jw, pk.shape[1]])
        p_perm = jnp.transpose(p5, perm + [3, 4]).reshape(pk.shape)
        part = lax.dot_general(p_perm, weight, (((1,), (0,)), ((), ())), preferred_element_type=jnp.float32) * (1.0 / M)
        x = part
        for a in order:
            x = rs(x, a, "pp")
        grams.append(x)
        g = x.astype(jnp.bfloat16)
        for a in reversed(order):
            g = ag(g, a, "pp")
        g5 = g.reshape([rshape[q] for q in perm] + [jw, g.shape[1]])
        gram_half = jnp.transpose(g5, inv + [3, 4]).reshape(g.shape)
        partial_t = lax.dot_general(gram_half, weight, (((1,), (1,)), ((), ())), preferred_element_type=jnp.float32)
        summed = rs(rs(partial_t, "x", "pp"), "yl", "pp")
        seg = summed.shape[0]
        own = lax.dynamic_slice_in_dim(pk, lax.axis_index(COL) * seg, seg, 0)
        upd = (1.5 * own.astype(jnp.float32) - 0.5 * summed).astype(jnp.bfloat16)
        upds.append(upd.reshape(n_row // n_col, jw, upd.shape[1]))
    gram_rows = jnp.concatenate(grams, 0) if chunks > 1 else grams[0]
    updated_t = jnp.stack(upds, 1).reshape(PANEL // n_col, own_block.shape[0])
    return (updated_t.T, gram_rows)


def solution(mesh):
    m5 = Mesh(mesh.devices.reshape(2, 8, 2, 4, 2), ROW + COL)
    return jax.shard_map(on_device, mesh=m5, in_specs=(P(ROW, COL), P()),
                         out_specs=(P(ROW, COL), P(ROW, COL)), check_vma=False)
```

```python
import jax
import jax.numpy as jnp
from jax import lax
from jax.sharding import PartitionSpec as P, Mesh

M = 16384
PANEL = 1024
CFG = {'chunks': 2, "order": ("c","z","yh"), "mode": {"c":"pp","z":"pp","yh":"pp"}}

ROW = ("yh", "z", "c")
COL = ("x", "yl")


def pair_rs(x, axis):
    k = lax.axis_index(axis)
    h = x.shape[0] // 2
    keep = lax.dynamic_slice_in_dim(x, k * h, h, 0)
    send = lax.dynamic_slice_in_dim(x, (1 - k) * h, h, 0)
    return keep + lax.ppermute(send, axis, [(0, 1), (1, 0)])


def pair_ag(x, axis):
    k = lax.axis_index(axis)
    got = lax.ppermute(x, axis, [(0, 1), (1, 0)])
    h = x.shape[0]
    out = lax.dynamic_update_slice_in_dim(jnp.zeros((2 * h,) + x.shape[1:], x.dtype), x, k * h, 0)
    return lax.dynamic_update_slice_in_dim(out, got, (1 - k) * h, 0)


def ring_rs(x, axis):
    n = lax.axis_size(axis)
    d = lax.axis_index(axis)
    h = x.shape[0] // n
    piece = lambda k: lax.dynamic_slice_in_dim(x, (k % n) * h, h, 0)
    fw = [(i, (i + 1) % n) for i in range(n)]
    bw = [(i, (i - 1) % n) for i in range(n)]
    ncw = n // 2
    nccw = n - 1 - ncw
    acc_cw = piece(d + ncw)
    acc_ccw = piece(d - nccw)
    for s in range(ncw):
        acc_cw = lax.ppermute(acc_cw, axis, fw)
        if s < nccw:
            acc_ccw = lax.ppermute(acc_ccw, axis, bw)
        if s < ncw - 1:
            acc_cw = acc_cw + piece(d + ncw - s - 1)
        if s < nccw - 1:
            acc_ccw = acc_ccw + piece(d - nccw + s + 1)
    return acc_cw + acc_ccw + piece(d)


def ring_ag(x, axis):
    n = lax.axis_size(axis)
    d = lax.axis_index(axis)
    h = x.shape[0]
    fw = [(i, (i + 1) % n) for i in range(n)]
    bw = [(i, (i - 1) % n) for i in range(n)]
    out = jnp.zeros((n * h,) + x.shape[1:], x.dtype)
    out = lax.dynamic_update_slice_in_dim(out, x, d * h, 0)
    ncw = n // 2
    nccw = n - 1 - ncw
    a = x
    b = x
    for s in range(ncw):
        a = lax.ppermute(a, axis, fw)
        out = lax.dynamic_update_slice_in_dim(out, a, ((d - s - 1) % n) * h, 0)
        if s < nccw:
            b = lax.ppermute(b, axis, bw)
            out = lax.dynamic_update_slice_in_dim(out, b, ((d + s + 1) % n) * h, 0)
    return out


def rs(x, axis, mode):
    if mode == "sc":
        return lax.psum_scatter(x, axis, scatter_dimension=0, tiled=True)
    if lax.axis_size(axis) == 2:
        return pair_rs(x, axis)
    return ring_rs(x, axis)


def ag(x, axis, mode):
    if mode == "sc":
        return lax.all_gather(x, axis, axis=0, tiled=True)
    if lax.axis_size(axis) == 2:
        return pair_ag(x, axis)
    return ring_ag(x, axis)


def broadcast_t(t, root):
    mine = lax.axis_index(COL) == root
    t = jnp.where(mine, t, jnp.zeros_like(t))
    t = rs(t, "x", "pp")
    t = rs(t, "yl", "pp")
    t = ag(t, "yl", "pp")
    return ag(t, "x", "pp")


def on_device(weight, panel_index):
    local_cols = weight.shape[1]
    begin_col = panel_index[0] * PANEL
    owner_col = begin_col // local_cols
    offset_col = begin_col % local_cols
    own_block = lax.dynamic_slice_in_dim(weight, offset_col, PANEL, 1)
    n_row = lax.axis_size(ROW)
    n_col = lax.axis_size(COL)
    rows_per = PANEL // n_row
    chunks = CFG["chunks"]
    jw = rows_per // chunks
    order = CFG["order"]
    sizes = {a: lax.axis_size(a) for a in ROW}
    perm = [ROW.index(a) for a in order]
    inv = [perm.index(q) for q in range(3)]
    rshape = [sizes[a] for a in ROW]
    blk = own_block.T.reshape(n_row, rows_per, own_block.shape[0])
    grams = []
    upds = []
    for k in range(chunks):
        pk = blk[:, k * jw:(k + 1) * jw, :].reshape(n_row * jw, own_block.shape[0])
        pk = broadcast_t(pk, owner_col)
        p5 = pk.reshape(rshape + [jw, pk.shape[1]])
        p_perm = jnp.transpose(p5, perm + [3, 4]).reshape(pk.shape)
        part = lax.dot_general(p_perm, weight, (((1,), (0,)), ((), ())), preferred_element_type=jnp.float32) * (1.0 / M)
        x = part
        for a in order:
            x = rs(x, a, "pp")
        grams.append(x)
        g = x.astype(jnp.bfloat16)
        for a in reversed(order):
            g = ag(g, a, "pp")
        g5 = g.reshape([rshape[q] for q in perm] + [jw, g.shape[1]])
        gram_half = jnp.transpose(g5, inv + [3, 4]).reshape(g.shape)
        partial_t = lax.dot_general(gram_half, weight, (((1,), (1,)), ((), ())), preferred_element_type=jnp.float32)
        summed = rs(rs(partial_t, "x", "pp"), "yl", "pp")
        seg = summed.shape[0]
        own = lax.dynamic_slice_in_dim(pk, lax.axis_index(COL) * seg, seg, 0)
        upd = (1.5 * own.astype(jnp.float32) - 0.5 * summed).astype(jnp.bfloat16)
        upds.append(upd.reshape(n_row // n_col, jw, upd.shape[1]))
    gram_rows = jnp.concatenate(grams, 0) if chunks > 1 else grams[0]
    updated_t = jnp.stack(upds, 1).reshape(PANEL // n_col, own_block.shape[0])
    return (updated_t.T, gram_rows)


def solution(mesh):
    m5 = Mesh(mesh.devices.reshape(2, 8, 2, 4, 2), ROW + COL)
    return jax.shard_map(on_device, mesh=m5, in_specs=(P(ROW, COL), P()),
                         out_specs=(P(ROW, COL), P(ROW, COL)), check_vma=False)
```

```python
import jax
import jax.numpy as jnp
from jax import lax
from jax.sharding import PartitionSpec as P, Mesh

M = 16384
PANEL = 1024
CFG = {'chunks': 2, "order": ("c","z","yh"), "mode": {"c":"pp","z":"pp","yh":"pp"}}

ROW = ("yh", "z", "c")
COL = ("x", "yl")


def pair_rs(x, axis):
    k = lax.axis_index(axis)
    h = x.shape[0] // 2
    keep = lax.dynamic_slice_in_dim(x, k * h, h, 0)
    send = lax.dynamic_slice_in_dim(x, (1 - k) * h, h, 0)
    return keep + lax.ppermute(send, axis, [(0, 1), (1, 0)])


def pair_ag(x, axis):
    k = lax.axis_index(axis)
    got = lax.ppermute(x, axis, [(0, 1), (1, 0)])
    h = x.shape[0]
    return lax.dynamic_update_slice_in_dim(jnp.concatenate([x, x], 0), got, (1 - k) * h, 0)


def ring_rs(x, axis):
    n = lax.axis_size(axis)
    d = lax.axis_index(axis)
    h = x.shape[0] // n
    piece = lambda k: lax.dynamic_slice_in_dim(x, (k % n) * h, h, 0)
    fw = [(i, (i + 1) % n) for i in range(n)]
    bw = [(i, (i - 1) % n) for i in range(n)]
    ncw = n // 2
    nccw = n - 1 - ncw
    acc_cw = piece(d + ncw)
    acc_ccw = piece(d - nccw)
    for s in range(ncw):
        acc_cw = lax.ppermute(acc_cw, axis, fw)
        if s < nccw:
            acc_ccw = lax.ppermute(acc_ccw, axis, bw)
        if s < ncw - 1:
            acc_cw = acc_cw + piece(d + ncw - s - 1)
        if s < nccw - 1:
            acc_ccw = acc_ccw + piece(d - nccw + s + 1)
    return acc_cw + acc_ccw + piece(d)


def ring_ag(x, axis):
    n = lax.axis_size(axis)
    d = lax.axis_index(axis)
    h = x.shape[0]
    fw = [(i, (i + 1) % n) for i in range(n)]
    bw = [(i, (i - 1) % n) for i in range(n)]
    out = jnp.concatenate([x] * n, 0)
    ncw = n // 2
    nccw = n - 1 - ncw
    a = x
    b = x
    for s in range(ncw):
        a = lax.ppermute(a, axis, fw)
        out = lax.dynamic_update_slice_in_dim(out, a, ((d - s - 1) % n) * h, 0)
        if s < nccw:
            b = lax.ppermute(b, axis, bw)
            out = lax.dynamic_update_slice_in_dim(out, b, ((d + s + 1) % n) * h, 0)
    return out


def rs(x, axis, mode):
    if mode == "sc":
        return lax.psum_scatter(x, axis, scatter_dimension=0, tiled=True)
    if lax.axis_size(axis) == 2:
        return pair_rs(x, axis)
    return ring_rs(x, axis)


def ag(x, axis, mode):
    if mode == "sc":
        return lax.all_gather(x, axis, axis=0, tiled=True)
    if lax.axis_size(axis) == 2:
        return pair_ag(x, axis)
    return ring_ag(x, axis)


def broadcast_t(t, root):
    mine = lax.axis_index(COL) == root
    t = jnp.where(mine, t, jnp.zeros_like(t))
    t = rs(t, "x", "pp")
    t = rs(t, "yl", "pp")
    t = ag(t, "yl", "pp")
    return ag(t, "x", "pp")


def on_device(weight, panel_index):
    local_cols = weight.shape[1]
    begin_col = panel_index[0] * PANEL
    owner_col = begin_col // local_cols
    offset_col = begin_col % local_cols
    own_block = lax.dynamic_slice_in_dim(weight, offset_col, PANEL, 1)
    n_row = lax.axis_size(ROW)
    n_col = lax.axis_size(COL)
    rows_per = PANEL // n_row
    chunks = CFG["chunks"]
    jw = rows_per // chunks
    order = CFG["order"]
    sizes = {a: lax.axis_size(a) for a in ROW}
    perm = [ROW.index(a) for a in order]
    inv = [perm.index(q) for q in range(3)]
    rshape = [sizes[a] for a in ROW]
    blk = own_block.T.reshape(n_row, rows_per, own_block.shape[0])
    grams = []
    upds = []
    for k in range(chunks):
        pk = blk[:, k * jw:(k + 1) * jw, :].reshape(n_row * jw, own_block.shape[0])
        pk = broadcast_t(pk, owner_col)
        p5 = pk.reshape(rshape + [jw, pk.shape[1]])
        p_perm = jnp.transpose(p5, perm + [3, 4]).reshape(pk.shape)
        part = lax.dot_general(p_perm, weight, (((1,), (0,)), ((), ())), preferred_element_type=jnp.float32) * (1.0 / M)
        x = part
        for a in order:
            x = rs(x, a, "pp")
        grams.append(x)
        g = x.astype(jnp.bfloat16)
        for a in reversed(order):
            g = ag(g, a, "pp")
        g5 = g.reshape([rshape[q] for q in perm] + [jw, g.shape[1]])
        gram_half = jnp.transpose(g5, inv + [3, 4]).reshape(g.shape)
        partial_t = lax.dot_general(gram_half, weight, (((1,), (1,)), ((), ())), preferred_element_type=jnp.float32)
        summed = rs(rs(partial_t, "x", "pp"), "yl", "pp")
        seg = summed.shape[0]
        own = lax.dynamic_slice_in_dim(pk, lax.axis_index(COL) * seg, seg, 0)
        upd = (1.5 * own.astype(jnp.float32) - 0.5 * summed).astype(jnp.bfloat16)
        upds.append(upd.reshape(n_row // n_col, jw, upd.shape[1]))
    gram_rows = jnp.concatenate(grams, 0) if chunks > 1 else grams[0]
    updated_t = jnp.stack(upds, 1).reshape(PANEL // n_col, own_block.shape[0])
    return (updated_t.T, gram_rows)


def solution(mesh):
    m5 = Mesh(mesh.devices.reshape(2, 8, 2, 4, 2), ROW + COL)
    return jax.shard_map(on_device, mesh=m5, in_specs=(P(ROW, COL), P()),
                         out_specs=(P(ROW, COL), P(ROW, COL)), check_vma=False)
```
